128 devices in a mesh: dp: 8 (over x_hi, z), row: 4 (over x_lo, core), col: 4 (over y).
Axes of the slice: x: 4 (x_hi: 2, x_lo: 2; x = x_hi * 2 + x_lo), y: 4, z: 4, core: 2. Of those that a mesh axis runs over, the one named last changes fastest.
Arguments:
- hidden_acts: bfloat16 [4096, 29568], P('dp', ('row', 'col')), may hold values from -6 to 6
- out_cotangent: bfloat16 [4096, 1024], P('dp'), may hold values from -6 to 6
- is_paraphrase: int32 [4096], P('dp'), may hold values 0 or 1
- token_edit: int32 [4096], P('dp'), may hold values from 0 to 511
- edit_weight: float32 [512], replicated, may hold values from 0.5 to 2
- inverse_gram: bfloat16 [29568, 29568], P(('row', 'col'), 'dp'), may hold values from -1 to 3
- edit_keys: bfloat16 [29568, 512], P('dp'), may hold values from -0.03125 to 0.03125
- edit_slots: int32 [512], replicated, may hold values from 0 to 511, each once
Outputs:
- edit_shift_grads: float32 [512, 1024], P('dp', ('row', 'col'))
The draws below stay inside these ranges and needn't reach their ends.
Inputs may be any that keep to these rules, and one draw needn't show every extreme that they name: `edit_slots`: every edit number appears in exactly one slot.
All inputs are finite; a program needn't handle non-finite values. No bound on the sum of `is_paraphrase` on one device may be relied on, other than what follows from the above.
Results may differ from the reference program's by a relative error of at most 0.024.
Values may be sent and summed in bfloat16 or wider, within the bound.
No kernel may reach another device: no remote copies, remote signals or barrier semaphores. Data moves between devices by JAX's collectives and lax.ppermute only.
A program may use at most 128 MiB of HBM per device.

```python
import math
import jax
import jax.numpy as jnp
from jax import lax

FF = 29568
ROWS = 1024
TOKENS = 4096
EDITS = 512
N_DP = 8


def draw_inverse_gram(key, part):
    noise_key = jax.random.fold_in(key, 11)
    diag_key = jax.random.fold_in(key, 23)
    row_index = lax.broadcasted_iota(jnp.int32, (FF, FF), 0)
    col_index = lax.broadcasted_iota(jnp.int32, (FF, FF), 1)
    noise = jnp.clip(jax.random.normal(noise_key, (FF, FF), jnp.float32), -3.0, 3.0) * (0.7 / math.sqrt(FF))
    diagonal = jax.random.uniform(diag_key, (FF,), jnp.float32, 1.0, 2.0)
    return (noise + jnp.where(row_index == col_index, diagonal[:, None], jnp.float32(0.0))).astype(jnp.bfloat16)


def place_ends(array, stream_key, smallest, top_value):
    longest = array.shape.index(max(array.shape))
    spots = []
    for shift in (0, 1):
        where = [jax.random.randint(jax.random.fold_in(stream_key, axis), (), 0, length) for axis, length in enumerate(array.shape)]
        where[longest] = (where[longest] + shift) % array.shape[longest]
        spots.append(tuple(where))
    return array.at[spots[0]].set(smallest).at[spots[1]].set(top_value)


def level_of(stream_key, dims, split, least, largest):
    gain = 1.0
    for dim, parts in split:
        draws = jax.random.uniform(jax.random.fold_in(jax.random.fold_in(stream_key, 6), dim), (parts,), jnp.float32, least / len(split), largest / len(split))
        gain = gain * jnp.repeat(jnp.exp(draws), dims[dim] // parts).reshape((-1,) + (1,) * (len(dims) - 1 - dim))
    return gain


def normal_values(own_key, dims, scale, most, pieces=(), kind=jnp.bfloat16):
    loudness = level_of(own_key, dims, pieces, -0.22, 0.18) if pieces else 1.0
    result = jax.random.normal(own_key, dims, jnp.float32) * scale * loudness
    return jnp.minimum(jnp.maximum(result, -most), most).astype(kind)


def setup_inputs(seed: int = 0) -> dict:
    streams_of = jax.random.split(jax.random.key(seed), 9)
    hidden_acts = normal_values(streams_of[0], (TOKENS, FF), 1.0, 6.0, ((0, 8), (1, 16)))
    out_cotangent = normal_values(streams_of[1], (TOKENS, ROWS), 1.0, 6.0, ((0, 8),))
    is_paraphrase = place_ends((jax.random.randint(streams_of[2], (TOKENS,), 0, 2) < 1).astype(jnp.int32), jax.random.fold_in(streams_of[2], 1), 0, 1)
    token_edit = place_ends(jax.random.randint(streams_of[3], (TOKENS,), 0, EDITS), jax.random.fold_in(streams_of[3], 1), 0, EDITS - 1).astype(jnp.int32)
    edit_weight = jnp.clip(jnp.exp(jax.random.uniform(streams_of[4], (EDITS,), jnp.float32, math.log(0.5), math.log(2.0))), 0.5, 2.0)
    inverse_gram = draw_inverse_gram(jax.random.fold_in(streams_of[8], 71), 0)
    edit_keys = normal_values(streams_of[6], (FF, EDITS), FF ** -0.5, 0.03125, ((0, 8),))
    edit_slots = jax.random.permutation(streams_of[7], EDITS).astype(jnp.int32)
    return dict(hidden_acts=hidden_acts, out_cotangent=out_cotangent, is_paraphrase=is_paraphrase, token_edit=token_edit, edit_weight=edit_weight, inverse_gram=inverse_gram, edit_keys=edit_keys, edit_slots=edit_slots)


def reference(hidden_acts, out_cotangent, is_paraphrase, token_edit, edit_weight, inverse_gram, edit_keys, edit_slots):
    tokens = hidden_acts.shape[0]
    looked = edit_weight[token_edit]
    weight = jnp.where(is_paraphrase == 1, looked, jnp.float32(1.0)) / jnp.sqrt(jnp.float32(tokens))
    scaled = (out_cotangent.astype(jnp.float32) * weight[:, None]).astype(jnp.bfloat16)
    grad_shift = lax.dot_general(scaled, hidden_acts, (((0,), (0,)), ((), ())), preferred_element_type=jnp.float32).astype(jnp.bfloat16)
    chosen = jnp.take(edit_keys, edit_slots, axis=1)
    width = FF // N_DP

    def add_block(carry, index):
        start = (index * width).astype(jnp.int32)
        columns = lax.dynamic_slice_in_dim(inverse_gram, start, width, 1)
        pushed = jnp.dot(grad_shift, columns, preferred_element_type=jnp.float32).astype(jnp.bfloat16)
        keys = lax.dynamic_slice_in_dim(chosen, start, width, 0)
        carry = carry + lax.dot_general(keys, pushed, (((0,), (1,)), ((), ())), preferred_element_type=jnp.float32)
        return (carry, None)
    initial = jnp.zeros((edit_slots.shape[0], grad_shift.shape[0]), jnp.float32)
    total, unused = lax.scan(add_block, initial, jnp.arange(N_DP, dtype=jnp.int32))
    return total
```

```python
import jax
import jax.numpy as jnp
from jax import lax
from jax.sharding import PartitionSpec as P


def body(
    hidden_acts,
    out_cotangent,
    is_paraphrase,
    token_edit,
    edit_weight,
    inverse_gram,
    edit_keys,
    edit_slots,
):
    tokens = hidden_acts.shape[0] * lax.axis_size("dp")
    edits = edit_weight.shape[0]
    match = token_edit[:, None] == jnp.arange(edits, dtype=jnp.int32)[None, :]
    looked = jnp.sum(jnp.where(match, edit_weight[None, :], jnp.float32(0.0)), axis=1)
    weight = jnp.where(is_paraphrase == 1, looked, jnp.float32(1.0)) / jnp.sqrt(jnp.float32(tokens))
    scaled = (out_cotangent.astype(jnp.float32) * weight[:, None]).astype(jnp.bfloat16)

    gram_keys = jnp.dot(inverse_gram, edit_keys, preferred_element_type=jnp.float32)
    gram_keys = lax.psum(gram_keys, "dp").astype(jnp.bfloat16)
    acts_keys = jnp.dot(hidden_acts, gram_keys, preferred_element_type=jnp.float32)
    acts_keys = lax.psum(acts_keys, ("row", "col"))
    rows = out_cotangent.shape[1] // (lax.axis_size("row") * lax.axis_size("col"))
    block = lax.axis_index("row") * lax.axis_size("col") + lax.axis_index("col")
    scaled_rows = lax.dynamic_slice_in_dim(scaled, block * rows, rows, axis=1)
    partial = lax.dot_general(
        acts_keys,
        scaled_rows.astype(jnp.float32),
        (((0,), (0,)), ((), ())),
        precision=lax.Precision.HIGHEST,
        preferred_element_type=jnp.float32,
    )
    partial = jnp.take(partial, edit_slots, axis=0)
    return lax.psum_scatter(partial, "dp", scatter_dimension=0, tiled=True)


def solution(mesh):
    return jax.shard_map(
        body,
        mesh=mesh,
        in_specs=(
            P("dp", ("row", "col")),
            P("dp", None),
            P("dp"),
            P("dp"),
            P(),
            P(("row", "col"), "dp"),
            P("dp", None),
            P(),
        ),
        out_specs=P("dp", ("row", "col")),
        check_vma=False,
    )
```

```python
import jax
import jax.numpy as jnp
from jax import lax
from jax.sharding import PartitionSpec as P


def reduce_scatter(x, axis, parts):
    pieces = x.reshape((parts, x.shape[0] // parts) + x.shape[1:])
    got = lax.all_to_all(pieces, axis, 0, 0)
    return jnp.sum(got.astype(jnp.float32), axis=0)


def all_gather(x, axis, parts):
    pieces = jnp.broadcast_to(x[None], (parts,) + x.shape)
    got = lax.all_to_all(pieces, axis, 0, 0)
    return got.reshape((parts * x.shape[0],) + x.shape[1:])


def body(
    hidden_acts,
    out_cotangent,
    is_paraphrase,
    token_edit,
    edit_weight,
    inverse_gram,
    edit_keys,
    edit_slots,
):
    n_dp = lax.axis_size("dp")
    n_rc = lax.axis_size("row") * lax.axis_size("col")
    tokens = hidden_acts.shape[0] * n_dp
    edits = edit_weight.shape[0]
    match = token_edit[:, None] == jnp.arange(edits, dtype=jnp.int32)[None, :]
    looked = jnp.sum(jnp.where(match, edit_weight[None, :], jnp.float32(0.0)), axis=1)
    weight = jnp.where(is_paraphrase == 1, looked, jnp.float32(1.0)) / jnp.sqrt(jnp.float32(tokens))
    scaled = (out_cotangent.astype(jnp.float32) * weight[:, None]).astype(jnp.bfloat16)

    gram_keys = jnp.dot(inverse_gram, edit_keys, preferred_element_type=jnp.float32)
    gram_keys = reduce_scatter(gram_keys.astype(jnp.bfloat16), "dp", n_dp)
    gram_keys = all_gather(gram_keys.astype(jnp.bfloat16), "dp", n_dp)
    acts_keys = jnp.dot(hidden_acts, gram_keys, preferred_element_type=jnp.float32)
    acts_keys = reduce_scatter(acts_keys.astype(jnp.bfloat16), ("row", "col"), n_rc)
    acts_keys = all_gather(acts_keys.astype(jnp.bfloat16), ("row", "col"), n_rc)
    rows = out_cotangent.shape[1] // n_rc
    block = lax.axis_index("row") * lax.axis_size("col") + lax.axis_index("col")
    scaled_rows = lax.dynamic_slice_in_dim(scaled, block * rows, rows, axis=1)
    partial = lax.dot_general(
        acts_keys, scaled_rows, (((0,), (0,)), ((), ())), preferred_element_type=jnp.float32
    )
    partial = jnp.take(partial, edit_slots, axis=0)
    return reduce_scatter(partial, "dp", n_dp)


def solution(mesh):
    return jax.shard_map(
        body,
        mesh=mesh,
        in_specs=(
            P("dp", ("row", "col")),
            P("dp", None),
            P("dp"),
            P("dp"),
            P(),
            P(("row", "col"), "dp"),
            P("dp", None),
            P(),
        ),
        out_specs=P("dp", ("row", "col")),
        check_vma=False,
    )
```

```python
import jax
import jax.numpy as jnp
from jax import lax
from jax.sharding import PartitionSpec as P


def reduce_scatter(x, axis, parts):
    pieces = x.reshape((parts, x.shape[0] // parts) + x.shape[1:])
    got = lax.all_to_all(pieces, axis, 0, 0)
    return jnp.sum(got.astype(jnp.float32), axis=0)


def all_gather(x, axis, parts):
    pieces = jnp.broadcast_to(x[None], (parts,) + x.shape)
    got = lax.all_to_all(pieces, axis, 0, 0)
    return got.reshape((parts * x.shape[0],) + x.shape[1:])


def body(
    hidden_acts,
    out_cotangent,
    is_paraphrase,
    token_edit,
    edit_weight,
    inverse_gram,
    edit_keys,
    edit_slots,
):
    n_dp = lax.axis_size("dp")
    n_rc = lax.axis_size("row") * lax.axis_size("col")
    tokens = hidden_acts.shape[0] * n_dp
    edits = edit_weight.shape[0]
    match = token_edit[:, None] == jnp.arange(edits, dtype=jnp.int32)[None, :]
    looked = jnp.sum(jnp.where(match, edit_weight[None, :], jnp.float32(0.0)), axis=1)
    weight = jnp.where(is_paraphrase == 1, looked, jnp.float32(1.0)) / jnp.sqrt(jnp.float32(tokens))
    scaled = (out_cotangent.astype(jnp.float32) * weight[:, None]).astype(jnp.bfloat16)

    gram_keys = jnp.dot(inverse_gram, edit_keys, preferred_element_type=jnp.float32)
    gram_keys = reduce_scatter(gram_keys.astype(jnp.bfloat16), "dp", n_dp)
    gram_keys = all_gather(gram_keys.astype(jnp.bfloat16), "dp", n_dp)
    acts_keys = jnp.dot(hidden_acts, gram_keys, preferred_element_type=jnp.float32)
    partial = lax.dot_general(
        scaled,
        acts_keys,
        (((0,), (0,)), ((), ())),
        precision=lax.Precision.HIGH,
        preferred_element_type=jnp.float32,
    )
    partial = reduce_scatter(partial.astype(jnp.bfloat16), ("row", "col"), n_rc)
    partial = jnp.take(partial.T, edit_slots, axis=0)
    return reduce_scatter(partial, "dp", n_dp)


def solution(mesh):
    return jax.shard_map(
        body,
        mesh=mesh,
        in_specs=(
            P("dp", ("row", "col")),
            P("dp", None),
            P("dp"),
            P("dp"),
            P(),
            P(("row", "col"), "dp"),
            P("dp", None),
            P(),
        ),
        out_specs=P("dp", ("row", "col")),
        check_vma=False,
    )
```

```python
import jax
import jax.numpy as jnp
from jax import lax
from jax.sharding import PartitionSpec as P


def reduce_scatter(x, axis, parts):
    pieces = x.reshape((parts, x.shape[0] // parts) + x.shape[1:])
    got = lax.all_to_all(pieces, axis, 0, 0)
    return jnp.sum(got.astype(jnp.float32), axis=0)


def all_gather(x, axis, parts):
    pieces = jnp.broadcast_to(x[None], (parts,) + x.shape)
    got = lax.all_to_all(pieces, axis, 0, 0)
    return got.reshape((parts * x.shape[0],) + x.shape[1:])


def body(
    hidden_acts,
    out_cotangent,
    is_paraphrase,
    token_edit,
    edit_weight,
    inverse_gram,
    edit_keys,
    edit_slots,
):
    n_dp = lax.axis_size("dp")
    n_rc = lax.axis_size("row") * lax.axis_size("col")
    tokens = hidden_acts.shape[0] * n_dp
    edits = edit_weight.shape[0]
    match = token_edit[:, None] == jnp.arange(edits, dtype=jnp.int32)[None, :]
    looked = jnp.sum(jnp.where(match, edit_weight[None, :], jnp.float32(0.0)), axis=1)
    weight = jnp.where(is_paraphrase == 1, looked, jnp.float32(1.0)) / jnp.sqrt(jnp.float32(tokens))
    scaled = (out_cotangent.astype(jnp.float32) * weight[:, None]).astype(jnp.bfloat16)

    rows = out_cotangent.shape[1] // n_rc
    halves = 2
    width = edits // halves
    pieces = []
    for h in range(halves):
        keys = edit_keys[:, h * width:(h + 1) * width]
        gram_keys = jnp.dot(inverse_gram, keys, preferred_element_type=jnp.float32)
        gram_keys = reduce_scatter(gram_keys.astype(jnp.bfloat16), "dp", n_dp)
        gram_keys = all_gather(gram_keys.astype(jnp.bfloat16), "dp", n_dp)
        acts_keys = jnp.dot(hidden_acts, gram_keys, preferred_element_type=jnp.float32)
        partial = lax.dot_general(
            scaled,
            acts_keys,
            (((0,), (0,)), ((), ())),
            precision=lax.Precision.HIGH,
            preferred_element_type=jnp.float32,
        )
        pieces.append(reduce_scatter(partial.astype(jnp.bfloat16), ("row", "col"), n_rc))
    partial = jnp.concatenate(pieces, axis=1)
    partial = jnp.take(partial.T, edit_slots, axis=0)
    return reduce_scatter(partial, "dp", n_dp)


def solution(mesh):
    return jax.shard_map(
        body,
        mesh=mesh,
        in_specs=(
            P("dp", ("row", "col")),
            P("dp", None),
            P("dp"),
            P("dp"),
            P(),
            P(("row", "col"), "dp"),
            P("dp", None),
            P(),
        ),
        out_specs=P("dp", ("row", "col")),
        check_vma=False,
    )
```

```python
import jax
import jax.numpy as jnp
from jax import lax
from jax.sharding import PartitionSpec as P


def reduce_scatter(x, axis, parts):
    pieces = x.reshape((parts, x.shape[0] // parts) + x.shape[1:])
    got = lax.all_to_all(pieces, axis, 0, 0)
    return jnp.sum(got.astype(jnp.float32), axis=0)


def all_gather(x, axis, parts):
    pieces = jnp.broadcast_to(x[None], (parts,) + x.shape)
    got = lax.all_to_all(pieces, axis, 0, 0)
    return got.reshape((parts * x.shape[0],) + x.shape[1:])


def body(
    hidden_acts,
    out_cotangent,
    is_paraphrase,
    token_edit,
    edit_weight,
    inverse_gram,
    edit_keys,
    edit_slots,
):
    n_dp = lax.axis_size("dp")
    n_rc = lax.axis_size("row") * lax.axis_size("col")
    tokens = hidden_acts.shape[0] * n_dp
    edits = edit_weight.shape[0]
    match = token_edit[:, None] == jnp.arange(edits, dtype=jnp.int32)[None, :]
    looked = jnp.sum(jnp.where(match, edit_weight[None, :], jnp.float32(0.0)), axis=1)
    weight = jnp.where(is_paraphrase == 1, looked, jnp.float32(1.0)) / jnp.sqrt(jnp.float32(tokens))
    scaled = (out_cotangent.astype(jnp.float32) * weight[:, None]).astype(jnp.bfloat16)

    gram_keys = jnp.dot(inverse_gram, edit_keys, preferred_element_type=jnp.float32)
    gram_keys = reduce_scatter(gram_keys.astype(jnp.bfloat16), "dp", n_dp)
    gram_keys = all_gather(gram_keys.astype(jnp.bfloat16), "dp", n_dp)
    acts_keys = jnp.dot(hidden_acts, gram_keys, preferred_element_type=jnp.float32)
    partial = lax.dot_general(
        acts_keys,
        scaled,
        (((0,), (0,)), ((), ())),
        precision=lax.Precision.HIGH,
        preferred_element_type=jnp.float32,
    )
    partial = jnp.take(partial.astype(jnp.bfloat16), edit_slots, axis=0)
    slots, cols = partial.shape
    blocks = partial.reshape(n_dp, slots // n_dp, n_rc, cols // n_rc).transpose(0, 2, 1, 3)
    blocks = blocks.reshape(n_dp * n_rc, slots // n_dp, cols // n_rc)
    return reduce_scatter(blocks.reshape(n_dp * n_rc * (slots // n_dp), cols // n_rc), ("dp", "row", "col"), n_dp * n_rc)


def solution(mesh):
    return jax.shard_map(
        body,
        mesh=mesh,
        in_specs=(
            P("dp", ("row", "col")),
            P("dp", None),
            P("dp"),
            P("dp"),
            P(),
            P(("row", "col"), "dp"),
            P("dp", None),
            P(),
        ),
        out_specs=P("dp", ("row", "col")),
        check_vma=False,
    )
```

```python
import jax
import jax.numpy as jnp
from jax import lax
from jax.sharding import PartitionSpec as P


def reduce_scatter(x, axis, parts):
    pieces = x.reshape((parts, x.shape[0] // parts) + x.shape[1:])
    got = lax.all_to_all(pieces, axis, 0, 0)
    return jnp.sum(got.astype(jnp.float32), axis=0)


def all_gather(x, axis, parts):
    pieces = jnp.broadcast_to(x[None], (parts,) + x.shape)
    got = lax.all_to_all(pieces, axis, 0, 0)
    return got.reshape((parts * x.shape[0],) + x.shape[1:])


def body(
    hidden_acts,
    out_cotangent,
    is_paraphrase,
    token_edit,
    edit_weight,
    inverse_gram,
    edit_keys,
    edit_slots,
):
    n_dp = lax.axis_size("dp")
    n_rc = lax.axis_size("row") * lax.axis_size("col")
    tokens = hidden_acts.shape[0] * n_dp
    edits = edit_weight.shape[0]
    match = token_edit[:, None] == jnp.arange(edits, dtype=jnp.int32)[None, :]
    looked = jnp.sum(jnp.where(match, edit_weight[None, :], jnp.float32(0.0)), axis=1)
    weight = jnp.where(is_paraphrase == 1, looked, jnp.float32(1.0)) / jnp.sqrt(jnp.float32(tokens))
    scaled = (out_cotangent.astype(jnp.float32) * weight[:, None]).astype(jnp.bfloat16)

    gram_keys = jnp.dot(inverse_gram, edit_keys, preferred_element_type=jnp.float32)
    gram_keys = reduce_scatter(gram_keys.astype(jnp.bfloat16), "dp", n_dp)
    gram_keys = all_gather(gram_keys.astype(jnp.bfloat16), "dp", n_dp)
    order = (jnp.arange(edits, dtype=jnp.int32)[:, None] == edit_slots[None, :]).astype(jnp.bfloat16)
    gram_keys = jnp.dot(gram_keys, order, preferred_element_type=jnp.float32).astype(jnp.bfloat16)
    acts_keys = jnp.dot(hidden_acts, gram_keys, preferred_element_type=jnp.float32)
    partial = lax.dot_general(
        acts_keys,
        scaled,
        (((0,), (0,)), ((), ())),
        precision=lax.Precision.HIGH,
        preferred_element_type=jnp.float32,
    )
    partial = partial.astype(jnp.bfloat16)
    slots, cols = partial.shape
    blocks = partial.reshape(n_dp, slots // n_dp, n_rc, cols // n_rc).transpose(0, 2, 1, 3)
    blocks = blocks.reshape(n_dp * n_rc, (slots // n_dp) * (cols // n_rc))
    got = lax.all_to_all(blocks, ("dp", "row", "col"), 0, 0)
    total = jnp.sum(got.astype(jnp.float32), axis=0)
    return total.reshape(slots // n_dp, cols // n_rc)


def solution(mesh):
    return jax.shard_map(
        body,
        mesh=mesh,
        in_specs=(
            P("dp", ("row", "col")),
            P("dp", None),
            P("dp"),
            P("dp"),
            P(),
            P(("row", "col"), "dp"),
            P("dp", None),
            P(),
        ),
        out_specs=P("dp", ("row", "col")),
        check_vma=False,
    )
```

```python
import jax
import jax.numpy as jnp
from jax import lax
from jax.sharding import PartitionSpec as P


Z_GROUPS = [[0, 1, 2, 3], [4, 5, 6, 7]]
X_GROUPS = [[0, 4], [1, 5], [2, 6], [3, 7]]


def reduce_scatter_dp(x):
    pieces = x.reshape((4, x.shape[0] // 4) + x.shape[1:])
    got = lax.all_to_all(pieces, "dp", 0, 0, axis_index_groups=Z_GROUPS)
    part = jnp.sum(got.astype(jnp.float32), axis=0).astype(jnp.bfloat16)
    pieces = part.reshape((2, part.shape[0] // 2) + part.shape[1:])
    got = lax.all_to_all(pieces, "dp", 0, 0, axis_index_groups=X_GROUPS)
    return jnp.sum(got.astype(jnp.float32), axis=0)


def all_gather_dp(x):
    got = lax.all_to_all(jnp.broadcast_to(x[None], (2,) + x.shape), "dp", 0, 0, axis_index_groups=X_GROUPS)
    part = got.reshape((2 * x.shape[0],) + x.shape[1:])
    got = lax.all_to_all(jnp.broadcast_to(part[None], (4,) + part.shape), "dp", 0, 0, axis_index_groups=Z_GROUPS)
    return got.reshape((4 * part.shape[0],) + part.shape[1:])


def reduce_scatter(x, axis, parts):
    pieces = x.reshape((parts, x.shape[0] // parts) + x.shape[1:])
    got = lax.all_to_all(pieces, axis, 0, 0)
    return jnp.sum(got.astype(jnp.float32), axis=0)


def all_gather(x, axis, parts):
    pieces = jnp.broadcast_to(x[None], (parts,) + x.shape)
    got = lax.all_to_all(pieces, axis, 0, 0)
    return got.reshape((parts * x.shape[0],) + x.shape[1:])


def body(
    hidden_acts,
    out_cotangent,
    is_paraphrase,
    token_edit,
    edit_weight,
    inverse_gram,
    edit_keys,
    edit_slots,
):
    n_dp = lax.axis_size("dp")
    n_rc = lax.axis_size("row") * lax.axis_size("col")
    tokens = hidden_acts.shape[0] * n_dp
    edits = edit_weight.shape[0]
    match = token_edit[:, None] == jnp.arange(edits, dtype=jnp.int32)[None, :]
    looked = jnp.sum(jnp.where(match, edit_weight[None, :], jnp.float32(0.0)), axis=1)
    weight = jnp.where(is_paraphrase == 1, looked, jnp.float32(1.0)) / jnp.sqrt(jnp.float32(tokens))
    scaled = (out_cotangent.astype(jnp.float32) * weight[:, None]).astype(jnp.bfloat16)

    gram_keys = jnp.dot(inverse_gram, edit_keys, preferred_element_type=jnp.float32)
    gram_keys = reduce_scatter_dp(gram_keys.astype(jnp.bfloat16))
    gram_keys = all_gather_dp(gram_keys.astype(jnp.bfloat16))
    acts_keys = jnp.dot(hidden_acts, gram_keys, preferred_element_type=jnp.float32)
    partial = lax.dot_general(
        scaled,
        acts_keys,
        (((0,), (0,)), ((), ())),
        precision=lax.Precision.HIGH,
        preferred_element_type=jnp.float32,
    )
    partial = reduce_scatter(partial.astype(jnp.bfloat16), ("row", "col"), n_rc)
    partial = jnp.take(partial.T, edit_slots, axis=0)
    return reduce_scatter(partial, "dp", n_dp)


def solution(mesh):
    return jax.shard_map(
        body,
        mesh=mesh,
        in_specs=(
            P("dp", ("row", "col")),
            P("dp", None),
            P("dp"),
            P("dp"),
            P(),
            P(("row", "col"), "dp"),
            P("dp", None),
            P(),
        ),
        out_specs=P("dp", ("row", "col")),
        check_vma=False,
    )
```

```python
import jax
import jax.numpy as jnp
from jax import lax
from jax.sharding import PartitionSpec as P


def reduce_scatter(x, axis, parts):
    pieces = x.reshape((parts, x.shape[0] // parts) + x.shape[1:])
    got = lax.all_to_all(pieces, axis, 0, 0)
    return jnp.sum(got.astype(jnp.float32), axis=0)


def all_gather(x, axis, parts):
    pieces = jnp.broadcast_to(x[None], (parts,) + x.shape)
    got = lax.all_to_all(pieces, axis, 0, 0)
    return got.reshape((parts * x.shape[0],) + x.shape[1:])


def body(
    hidden_acts,
    out_cotangent,
    is_paraphrase,
    token_edit,
    edit_weight,
    inverse_gram,
    edit_keys,
    edit_slots,
):
    n_dp = lax.axis_size("dp")
    n_rc = lax.axis_size("row") * lax.axis_size("col")
    tokens = hidden_acts.shape[0] * n_dp
    edits = edit_weight.shape[0]
    match = token_edit[:, None] == jnp.arange(edits, dtype=jnp.int32)[None, :]
    looked = jnp.sum(jnp.where(match, edit_weight[None, :], jnp.float32(0.0)), axis=1)
    weight = jnp.where(is_paraphrase == 1, looked, jnp.float32(1.0)) / jnp.sqrt(jnp.float32(tokens))
    scaled = (out_cotangent.astype(jnp.float32) * weight[:, None]).astype(jnp.bfloat16)

    gram_keys = jnp.dot(inverse_gram, edit_keys, preferred_element_type=jnp.float32)
    gram_keys = reduce_scatter(gram_keys.astype(jnp.bfloat16), "dp", n_dp)
    gram_keys = all_gather(gram_keys.astype(jnp.bfloat16), "dp", n_dp)
    order = (jnp.arange(edits, dtype=jnp.int32)[:, None] == edit_slots[None, :]).astype(jnp.bfloat16)
    gram_keys = jnp.dot(gram_keys, order, preferred_element_type=jnp.float32).astype(jnp.bfloat16)
    acts_keys = jnp.dot(hidden_acts, gram_keys, preferred_element_type=jnp.float32)
    slots = acts_keys.shape[1]
    cols = scaled.shape[1]
    partial = lax.dot_general(
        scaled,
        acts_keys.reshape(acts_keys.shape[0], n_dp, slots // n_dp),
        (((0,), (0,)), ((), ())),
        precision=lax.Precision.HIGH,
        preferred_element_type=jnp.float32,
    )
    blocks = partial.astype(jnp.bfloat16).transpose(1, 0, 2)
    blocks = blocks.reshape(n_dp * n_rc, 2, (cols // n_rc) * (slots // n_dp) // 2)
    got = lax.all_to_all(blocks, ("dp", "row", "col"), 0, 0)
    total = jnp.sum(got.astype(jnp.float32), axis=0)
    return total.reshape(cols // n_rc, slots // n_dp).T


def solution(mesh):
    return jax.shard_map(
        body,
        mesh=mesh,
        in_specs=(
            P("dp", ("row", "col")),
            P("dp", None),
            P("dp"),
            P("dp"),
            P(),
            P(("row", "col"), "dp"),
            P("dp", None),
            P(),
        ),
        out_specs=P("dp", ("row", "col")),
        check_vma=False,
    )
```

```python
import jax
import jax.numpy as jnp
from jax import lax
from jax.sharding import PartitionSpec as P


def reduce_scatter(x, axis, parts):
    pieces = x.reshape((parts, x.shape[0] // parts) + x.shape[1:])
    got = lax.all_to_all(pieces, axis, 0, 0)
    return jnp.sum(got.astype(jnp.float32), axis=0)


def all_gather(x, axis, parts):
    pieces = jnp.broadcast_to(x[None], (parts,) + x.shape)
    got = lax.all_to_all(pieces, axis, 0, 0)
    return got.reshape((parts * x.shape[0],) + x.shape[1:])


def body(
    hidden_acts,
    out_cotangent,
    is_paraphrase,
    token_edit,
    edit_weight,
    inverse_gram,
    edit_keys,
    edit_slots,
):
    n_dp = lax.axis_size("dp")
    n_rc = lax.axis_size("row") * lax.axis_size("col")
    tokens = hidden_acts.shape[0] * n_dp
    edits = edit_weight.shape[0]
    match = token_edit[:, None] == jnp.arange(edits, dtype=jnp.int32)[None, :]
    looked = jnp.sum(jnp.where(match, edit_weight[None, :], jnp.float32(0.0)), axis=1)
    weight = jnp.where(is_paraphrase == 1, looked, jnp.float32(1.0)) / jnp.sqrt(jnp.float32(tokens))
    scaled = (out_cotangent.astype(jnp.float32) * weight[:, None]).astype(jnp.bfloat16)

    gram_keys = jnp.dot(inverse_gram, edit_keys, preferred_element_type=jnp.float32)
    gram_keys = reduce_scatter(gram_keys.astype(jnp.bfloat16), "dp", n_dp)
    gram_keys = all_gather(gram_keys.astype(jnp.bfloat16), "dp", n_dp)
    order = (jnp.arange(edits, dtype=jnp.int32)[:, None] == edit_slots[None, :]).astype(jnp.bfloat16)
    gram_keys = jnp.dot(gram_keys, order, preferred_element_type=jnp.float32).astype(jnp.bfloat16)
    acts_keys = jnp.dot(hidden_acts, gram_keys, preferred_element_type=jnp.float32)
    slots = acts_keys.shape[1]
    cols = scaled.shape[1]
    partial = lax.dot_general(
        scaled,
        acts_keys.reshape(acts_keys.shape[0], n_dp, slots // n_dp),
        (((0,), (0,)), ((), ())),
        precision=lax.Precision.HIGH,
        preferred_element_type=jnp.float32,
    )
    blocks = partial.astype(jnp.bfloat16).transpose(1, 0, 2)
    blocks = blocks.reshape(n_dp * n_rc, 2, (cols // n_rc) * (slots // n_dp) // 2)
    n_row, n_col = lax.axis_size("row"), lax.axis_size("col")
    core = lax.axis_index("row") % 2
    split = blocks.reshape((n_dp, n_row // 2, 2, n_col) + blocks.shape[1:])
    mine = jnp.take(split, core, axis=2)
    other = jnp.take(split, 1 - core, axis=2)
    other = lax.ppermute(other, "row", [(r, r ^ 1) for r in range(n_row)])
    summed = (mine.astype(jnp.float32) + other.astype(jnp.float32)).astype(jnp.bfloat16)
    summed = summed.reshape((n_dp * n_rc // 2,) + blocks.shape[1:])
    groups = [[m for m in range(n_dp * n_rc) if (m // n_col) % 2 == c] for c in range(2)]
    got = lax.all_to_all(summed, ("dp", "row", "col"), 0, 0, axis_index_groups=groups)
    total = jnp.sum(got.astype(jnp.float32), axis=0)
    return total.reshape(cols // n_rc, slots // n_dp).T


def solution(mesh):
    return jax.shard_map(
        body,
        mesh=mesh,
        in_specs=(
            P("dp", ("row", "col")),
            P("dp", None),
            P("dp"),
            P("dp"),
            P(),
            P(("row", "col"), "dp"),
            P("dp", None),
            P(),
        ),
        out_specs=P("dp", ("row", "col")),
        check_vma=False,
    )
```

```python
import jax
import jax.numpy as jnp
from jax import lax
from jax.sharding import PartitionSpec as P


def reduce_scatter(x, axis, parts):
    pieces = x.reshape((parts, x.shape[0] // parts) + x.shape[1:])
    got = lax.all_to_all(pieces, axis, 0, 0)
    return jnp.sum(got.astype(jnp.float32), axis=0)


def all_gather(x, axis, parts):
    pieces = jnp.broadcast_to(x[None], (parts,) + x.shape)
    got = lax.all_to_all(pieces, axis, 0, 0)
    return got.reshape((parts * x.shape[0],) + x.shape[1:])


def body(
    hidden_acts,
    out_cotangent,
    is_paraphrase,
    token_edit,
    edit_weight,
    inverse_gram,
    edit_keys,
    edit_slots,
):
    n_dp = lax.axis_size("dp")
    n_rc = lax.axis_size("row") * lax.axis_size("col")
    tokens = hidden_acts.shape[0] * n_dp
    edits = edit_weight.shape[0]
    match = token_edit[:, None] == jnp.arange(edits, dtype=jnp.int32)[None, :]
    looked = jnp.sum(jnp.where(match, edit_weight[None, :], jnp.float32(0.0)), axis=1)
    weight = jnp.where(is_paraphrase == 1, looked, jnp.float32(1.0)) / jnp.sqrt(jnp.float32(tokens))
    scaled = (out_cotangent.astype(jnp.float32) * weight[:, None]).astype(jnp.bfloat16)

    gram_keys = jnp.dot(inverse_gram, edit_keys, preferred_element_type=jnp.float32)
    gram_keys = reduce_scatter(gram_keys.astype(jnp.bfloat16), "dp", n_dp)
    gram_keys = gram_keys.astype(jnp.bfloat16)
    gathered = lax.all_to_all(jnp.broadcast_to(gram_keys[None], (n_dp,) + gram_keys.shape), "dp", 0, 0)
    order = (jnp.arange(edits, dtype=jnp.int32)[:, None] == edit_slots[None, :]).astype(jnp.bfloat16)
    gathered = jnp.dot(gathered, order, preferred_element_type=jnp.float32).astype(jnp.bfloat16)
    acts = hidden_acts.reshape(hidden_acts.shape[0], n_dp, hidden_acts.shape[1] // n_dp)
    acts_keys = lax.dot_general(acts, gathered, (((1, 2), (0, 1)), ((), ())), preferred_element_type=jnp.float32)
    slots = acts_keys.shape[1]
    cols = scaled.shape[1]
    partial = lax.dot_general(
        scaled,
        acts_keys.reshape(acts_keys.shape[0], n_dp, slots // n_dp),
        (((0,), (0,)), ((), ())),
        precision=lax.Precision.HIGH,
        preferred_element_type=jnp.float32,
    )
    blocks = partial.astype(jnp.bfloat16).transpose(1, 0, 2)
    blocks = blocks.reshape(n_dp * n_rc, 2, (cols // n_rc) * (slots // n_dp) // 2)
    got = lax.all_to_all(blocks, ("dp", "row", "col"), 0, 0)
    total = jnp.sum(got.astype(jnp.float32), axis=0)
    return total.reshape(cols // n_rc, slots // n_dp).T


def solution(mesh):
    return jax.shard_map(
        body,
        mesh=mesh,
        in_specs=(
            P("dp", ("row", "col")),
            P("dp", None),
            P("dp"),
            P("dp"),
            P(),
            P(("row", "col"), "dp"),
            P("dp", None),
            P(),
        ),
        out_specs=P("dp", ("row", "col")),
        check_vma=False,
    )
```

```python
import jax
import jax.numpy as jnp
from jax import lax
from jax.sharding import PartitionSpec as P


def reduce_scatter(x, axis, parts):
    pieces = x.reshape((parts, x.shape[0] // parts) + x.shape[1:])
    got = lax.all_to_all(pieces, axis, 0, 0)
    return jnp.sum(got.astype(jnp.float32), axis=0)


def all_gather(x, axis, parts):
    pieces = jnp.broadcast_to(x[None], (parts,) + x.shape)
    got = lax.all_to_all(pieces, axis, 0, 0)
    return got.reshape((parts * x.shape[0],) + x.shape[1:])


def body(
    hidden_acts,
    out_cotangent,
    is_paraphrase,
    token_edit,
    edit_weight,
    inverse_gram,
    edit_keys,
    edit_slots,
):
    n_dp = lax.axis_size("dp")
    n_rc = lax.axis_size("row") * lax.axis_size("col")
    tokens = hidden_acts.shape[0] * n_dp
    edits = edit_weight.shape[0]
    match = token_edit[:, None] == jnp.arange(edits, dtype=jnp.int32)[None, :]
    looked = jnp.sum(jnp.where(match, edit_weight[None, :], jnp.float32(0.0)), axis=1)
    weight = jnp.where(is_paraphrase == 1, looked, jnp.float32(1.0)) / jnp.sqrt(jnp.float32(tokens))
    scaled = (out_cotangent.astype(jnp.float32) * weight[:, None]).astype(jnp.bfloat16)

    gram_keys = jnp.dot(inverse_gram, edit_keys, preferred_element_type=jnp.float32)
    gram_keys = reduce_scatter(gram_keys.astype(jnp.bfloat16), "dp", n_dp)
    order = (jnp.arange(edits, dtype=jnp.int32)[:, None] == edit_slots[None, :]).astype(jnp.bfloat16)
    gram_keys = jnp.dot(gram_keys.astype(jnp.bfloat16), order, preferred_element_type=jnp.float32).astype(jnp.bfloat16)
    gathered = lax.all_to_all(jnp.broadcast_to(gram_keys[None], (n_dp,) + gram_keys.shape), "dp", 0, 0)
    acts = hidden_acts.reshape(hidden_acts.shape[0], n_dp, hidden_acts.shape[1] // n_dp)
    acts_keys = lax.dot_general(acts, gathered, (((1, 2), (0, 1)), ((), ())), preferred_element_type=jnp.float32)
    slots = acts_keys.shape[1]
    cols = scaled.shape[1]
    partial = lax.dot_general(
        scaled,
        acts_keys.reshape(acts_keys.shape[0], n_dp, slots // n_dp),
        (((0,), (0,)), ((), ())),
        precision=lax.Precision.HIGH,
        preferred_element_type=jnp.float32,
    )
    blocks = partial.astype(jnp.bfloat16).transpose(1, 0, 2)
    blocks = blocks.reshape(n_dp * n_rc, 2, (cols // n_rc) * (slots // n_dp) // 2)
    got = lax.all_to_all(blocks, ("dp", "row", "col"), 0, 0)
    total = jnp.sum(got.astype(jnp.float32), axis=0)
    return total.reshape(cols // n_rc, slots // n_dp).T


def solution(mesh):
    return jax.shard_map(
        body,
        mesh=mesh,
        in_specs=(
            P("dp", ("row", "col")),
            P("dp", None),
            P("dp"),
            P("dp"),
            P(),
            P(("row", "col"), "dp"),
            P("dp", None),
            P(),
        ),
        out_specs=P("dp", ("row", "col")),
        check_vma=False,
    )
```

```python
import jax
import jax.numpy as jnp
from jax import lax
from jax.sharding import PartitionSpec as P


def reduce_scatter(x, axis, parts):
    pieces = x.reshape((parts, x.shape[0] // parts) + x.shape[1:])
    got = lax.all_to_all(pieces, axis, 0, 0)
    return jnp.sum(got.astype(jnp.float32), axis=0)


def all_gather(x, axis, parts):
    pieces = jnp.broadcast_to(x[None], (parts,) + x.shape)
    got = lax.all_to_all(pieces, axis, 0, 0)
    return got.reshape((parts * x.shape[0],) + x.shape[1:])


def body(
    hidden_acts,
    out_cotangent,
    is_paraphrase,
    token_edit,
    edit_weight,
    inverse_gram,
    edit_keys,
    edit_slots,
):
    n_dp = lax.axis_size("dp")
    n_rc = lax.axis_size("row") * lax.axis_size("col")
    tokens = hidden_acts.shape[0] * n_dp
    edits = edit_weight.shape[0]
    match = token_edit[:, None] == jnp.arange(edits, dtype=jnp.int32)[None, :]
    looked = jnp.sum(jnp.where(match, edit_weight[None, :], jnp.float32(0.0)), axis=1)
    weight = jnp.where(is_paraphrase == 1, looked, jnp.float32(1.0)) / jnp.sqrt(jnp.float32(tokens))
    scaled = (out_cotangent.astype(jnp.float32) * weight[:, None]).astype(jnp.bfloat16)

    ff = inverse_gram.shape[0]
    first = (ff // n_dp) // 2 // 16 * 16 * n_dp
    chunks = ((0, first), (first, ff))
    reduced = []
    for lo, hi in chunks:
        part = jnp.dot(inverse_gram[lo:hi], edit_keys, preferred_element_type=jnp.float32)
        reduced.append(reduce_scatter(part.astype(jnp.bfloat16), "dp", n_dp))
    gram_keys = jnp.concatenate(reduced, axis=0)
    order = (jnp.arange(edits, dtype=jnp.int32)[:, None] == edit_slots[None, :]).astype(jnp.bfloat16)
    gram_keys = jnp.dot(gram_keys.astype(jnp.bfloat16), order, preferred_element_type=jnp.float32).astype(jnp.bfloat16)
    gathered = lax.all_to_all(jnp.broadcast_to(gram_keys[None], (n_dp,) + gram_keys.shape), "dp", 0, 0)
    acts = jnp.concatenate(
        [hidden_acts[:, lo:hi].reshape(hidden_acts.shape[0], n_dp, (hi - lo) // n_dp) for lo, hi in chunks], axis=2
    )
    acts_keys = lax.dot_general(acts, gathered, (((1, 2), (0, 1)), ((), ())), preferred_element_type=jnp.float32)
    slots = acts_keys.shape[1]
    cols = scaled.shape[1]
    partial = lax.dot_general(
        scaled,
        acts_keys.reshape(acts_keys.shape[0], n_dp, slots // n_dp),
        (((0,), (0,)), ((), ())),
        precision=lax.Precision.HIGH,
        preferred_element_type=jnp.float32,
    )
    blocks = partial.astype(jnp.bfloat16).transpose(1, 0, 2)
    blocks = blocks.reshape(n_dp * n_rc, 2, (cols // n_rc) * (slots // n_dp) // 2)
    got = lax.all_to_all(blocks, ("dp", "row", "col"), 0, 0)
    total = jnp.sum(got.astype(jnp.float32), axis=0)
    return total.reshape(cols // n_rc, slots // n_dp).T


def solution(mesh):
    return jax.shard_map(
        body,
        mesh=mesh,
        in_specs=(
            P("dp", ("row", "col")),
            P("dp", None),
            P("dp"),
            P("dp"),
            P(),
            P(("row", "col"), "dp"),
            P("dp", None),
            P(),
        ),
        out_specs=P("dp", ("row", "col")),
        check_vma=False,
    )
```

```python
import jax
import jax.numpy as jnp
from jax import lax
from jax.sharding import PartitionSpec as P


def reduce_scatter(x, axis, parts):
    pieces = x.reshape((parts, x.shape[0] // parts) + x.shape[1:])
    got = lax.all_to_all(pieces, axis, 0, 0)
    return jnp.sum(got.astype(jnp.float32), axis=0)


def all_gather(x, axis, parts):
    pieces = jnp.broadcast_to(x[None], (parts,) + x.shape)
    got = lax.all_to_all(pieces, axis, 0, 0)
    return got.reshape((parts * x.shape[0],) + x.shape[1:])


def body(
    hidden_acts,
    out_cotangent,
    is_paraphrase,
    token_edit,
    edit_weight,
    inverse_gram,
    edit_keys,
    edit_slots,
):
    n_dp = lax.axis_size("dp")
    n_rc = lax.axis_size("row") * lax.axis_size("col")
    tokens = hidden_acts.shape[0] * n_dp
    edits = edit_weight.shape[0]
    match = token_edit[:, None] == jnp.arange(edits, dtype=jnp.int32)[None, :]
    looked = jnp.sum(jnp.where(match, edit_weight[None, :], jnp.float32(0.0)), axis=1)
    weight = jnp.where(is_paraphrase == 1, looked, jnp.float32(1.0)) / jnp.sqrt(jnp.float32(tokens))
    scaled = (out_cotangent.astype(jnp.float32) * weight[:, None]).astype(jnp.bfloat16)

    gram_keys = jnp.dot(inverse_gram, edit_keys, preferred_element_type=jnp.float32)
    gram_keys = reduce_scatter(gram_keys.astype(jnp.bfloat16), "dp", n_dp)
    order = (jnp.arange(edits, dtype=jnp.int32)[:, None] == edit_slots[None, :]).astype(jnp.bfloat16)
    gram_keys = jnp.dot(gram_keys.astype(jnp.bfloat16), order, preferred_element_type=jnp.float32).astype(jnp.bfloat16)
    gathered = lax.all_to_all(jnp.broadcast_to(gram_keys[None], (n_dp,) + gram_keys.shape), "dp", 0, 0)
    acts = hidden_acts.reshape(hidden_acts.shape[0], n_dp, hidden_acts.shape[1] // n_dp)
    acts_keys = lax.dot_general(acts, gathered, (((1, 2), (0, 1)), ((), ())), preferred_element_type=jnp.float32)
    slots = acts_keys.shape[1]
    cols = scaled.shape[1]
    partial = lax.dot_general(
        scaled,
        acts_keys.astype(jnp.bfloat16).reshape(acts_keys.shape[0], n_dp, slots // n_dp),
        (((0,), (0,)), ((), ())),
        preferred_element_type=jnp.float32,
    )
    blocks = partial.astype(jnp.bfloat16).transpose(1, 0, 2)
    blocks = blocks.reshape(n_dp * n_rc, 2, (cols // n_rc) * (slots // n_dp) // 2)
    got = lax.all_to_all(blocks, ("dp", "row", "col"), 0, 0)
    total = jnp.sum(got.astype(jnp.float32), axis=0)
    return total.reshape(cols // n_rc, slots // n_dp).T


def solution(mesh):
    return jax.shard_map(
        body,
        mesh=mesh,
        in_specs=(
            P("dp", ("row", "col")),
            P("dp", None),
            P("dp"),
            P("dp"),
            P(),
            P(("row", "col"), "dp"),
            P("dp", None),
            P(),
        ),
        out_specs=P("dp", ("row", "col")),
        check_vma=False,
    )
```

```python
import jax
import jax.numpy as jnp
from jax import lax
from jax.experimental import pallas as pl
from jax.sharding import PartitionSpec as P


def gram_keys_kernel(g_ref, k_ref, o_ref):
    o_ref[...] = jnp.dot(g_ref[...], k_ref[...], preferred_element_type=jnp.float32).astype(o_ref.dtype)


def gram_times_keys(gram, keys, block_rows):
    rows, inner = gram.shape
    width = keys.shape[1]
    return pl.pallas_call(
        gram_keys_kernel,
        grid=(rows // block_rows,),
        in_specs=[
            pl.BlockSpec((block_rows, inner), lambda i: (i, 0)),
            pl.BlockSpec((inner, width), lambda i: (0, 0)),
        ],
        out_specs=pl.BlockSpec((block_rows, width), lambda i: (i, 0)),
        out_shape=jax.ShapeDtypeStruct((rows, width), jnp.bfloat16),
        cost_estimate=pl.CostEstimate(
            flops=2 * rows * inner * width,
            bytes_accessed=2 * (rows * inner + inner * width + rows * width),
            transcendentals=0,
        ),
    )(gram, keys)


def reduce_scatter(x, axis, parts):
    pieces = x.reshape((parts, x.shape[0] // parts) + x.shape[1:])
    got = lax.all_to_all(pieces, axis, 0, 0)
    return jnp.sum(got.astype(jnp.float32), axis=0)


def all_gather(x, axis, parts):
    pieces = jnp.broadcast_to(x[None], (parts,) + x.shape)
    got = lax.all_to_all(pieces, axis, 0, 0)
    return got.reshape((parts * x.shape[0],) + x.shape[1:])


def body(
    hidden_acts,
    out_cotangent,
    is_paraphrase,
    token_edit,
    edit_weight,
    inverse_gram,
    edit_keys,
    edit_slots,
):
    n_dp = lax.axis_size("dp")
    n_rc = lax.axis_size("row") * lax.axis_size("col")
    tokens = hidden_acts.shape[0] * n_dp
    edits = edit_weight.shape[0]
    match = token_edit[:, None] == jnp.arange(edits, dtype=jnp.int32)[None, :]
    looked = jnp.sum(jnp.where(match, edit_weight[None, :], jnp.float32(0.0)), axis=1)
    weight = jnp.where(is_paraphrase == 1, looked, jnp.float32(1.0)) / jnp.sqrt(jnp.float32(tokens))
    scaled = (out_cotangent.astype(jnp.float32) * weight[:, None]).astype(jnp.bfloat16)

    gram_keys = gram_times_keys(inverse_gram, edit_keys, inverse_gram.shape[0] // 7)
    gram_keys = reduce_scatter(gram_keys.astype(jnp.bfloat16), "dp", n_dp)
    order = (jnp.arange(edits, dtype=jnp.int32)[:, None] == edit_slots[None, :]).astype(jnp.bfloat16)
    gram_keys = jnp.dot(gram_keys.astype(jnp.bfloat16), order, preferred_element_type=jnp.float32).astype(jnp.bfloat16)
    gathered = lax.all_to_all(jnp.broadcast_to(gram_keys[None], (n_dp,) + gram_keys.shape), "dp", 0, 0)
    acts = hidden_acts.reshape(hidden_acts.shape[0], n_dp, hidden_acts.shape[1] // n_dp)
    acts_keys = lax.dot_general(acts, gathered, (((1, 2), (0, 1)), ((), ())), preferred_element_type=jnp.float32)
    slots = acts_keys.shape[1]
    cols = scaled.shape[1]
    partial = lax.dot_general(
        scaled,
        acts_keys.reshape(acts_keys.shape[0], n_dp, slots // n_dp),
        (((0,), (0,)), ((), ())),
        precision=lax.Precision.HIGH,
        preferred_element_type=jnp.float32,
    )
    blocks = partial.astype(jnp.bfloat16).transpose(1, 0, 2)
    blocks = blocks.reshape(n_dp * n_rc, 2, (cols // n_rc) * (slots // n_dp) // 2)
    got = lax.all_to_all(blocks, ("dp", "row", "col"), 0, 0)
    total = jnp.sum(got.astype(jnp.float32), axis=0)
    return total.reshape(cols // n_rc, slots // n_dp).T


def solution(mesh):
    return jax.shard_map(
        body,
        mesh=mesh,
        in_specs=(
            P("dp", ("row", "col")),
            P("dp", None),
            P("dp"),
            P("dp"),
            P(),
            P(("row", "col"), "dp"),
            P("dp", None),
            P(),
        ),
        out_specs=P("dp", ("row", "col")),
        check_vma=False,
    )
```

```python
import jax
import jax.numpy as jnp
from jax import lax
from jax.sharding import PartitionSpec as P


def reduce_scatter(x, axis, parts):
    pieces = x.reshape((parts, x.shape[0] // parts) + x.shape[1:])
    got = lax.all_to_all(pieces, axis, 0, 0)
    return jnp.sum(got.astype(jnp.float32), axis=0)


def all_gather(x, axis, parts):
    pieces = jnp.broadcast_to(x[None], (parts,) + x.shape)
    got = lax.all_to_all(pieces, axis, 0, 0)
    return got.reshape((parts * x.shape[0],) + x.shape[1:])


def body(
    hidden_acts,
    out_cotangent,
    is_paraphrase,
    token_edit,
    edit_weight,
    inverse_gram,
    edit_keys,
    edit_slots,
):
    n_dp = lax.axis_size("dp")
    n_rc = lax.axis_size("row") * lax.axis_size("col")
    tokens = hidden_acts.shape[0] * n_dp
    edits = edit_weight.shape[0]
    match = token_edit[:, None] == jnp.arange(edits, dtype=jnp.int32)[None, :]
    looked = jnp.sum(jnp.where(match, edit_weight[None, :], jnp.float32(0.0)), axis=1)
    weight = jnp.where(is_paraphrase == 1, looked, jnp.float32(1.0)) / jnp.sqrt(jnp.float32(tokens))
    scaled = (out_cotangent.astype(jnp.float32) * weight[:, None]).astype(jnp.bfloat16)

    gram_keys = jnp.dot(inverse_gram, edit_keys, preferred_element_type=jnp.float32)
    gram_keys = reduce_scatter(gram_keys.astype(jnp.bfloat16), "dp", n_dp)
    acts = hidden_acts.reshape(hidden_acts.shape[0], n_dp, hidden_acts.shape[1] // n_dp)
    acts, gram_keys = lax.optimization_barrier((acts, gram_keys))
    order = (jnp.arange(edits, dtype=jnp.int32)[:, None] == edit_slots[None, :]).astype(jnp.bfloat16)
    gram_keys = jnp.dot(gram_keys.astype(jnp.bfloat16), order, preferred_element_type=jnp.float32).astype(jnp.bfloat16)
    gathered = lax.all_to_all(jnp.broadcast_to(gram_keys[None], (n_dp,) + gram_keys.shape), "dp", 0, 0)
    acts_keys = lax.dot_general(acts, gathered, (((1, 2), (0, 1)), ((), ())), preferred_element_type=jnp.float32)
    slots = acts_keys.shape[1]
    cols = scaled.shape[1]
    partial = lax.dot_general(
        scaled,
        acts_keys.reshape(acts_keys.shape[0], n_dp, slots // n_dp),
        (((0,), (0,)), ((), ())),
        precision=lax.Precision.HIGH,
        preferred_element_type=jnp.float32,
    )
    blocks = partial.astype(jnp.bfloat16).transpose(1, 0, 2)
    blocks = blocks.reshape(n_dp * n_rc, 2, (cols // n_rc) * (slots // n_dp) // 2)
    got = lax.all_to_all(blocks, ("dp", "row", "col"), 0, 0)
    total = jnp.sum(got.astype(jnp.float32), axis=0)
    return total.reshape(cols // n_rc, slots // n_dp).T


def solution(mesh):
    return jax.shard_map(
        body,
        mesh=mesh,
        in_specs=(
            P("dp", ("row", "col")),
            P("dp", None),
            P("dp"),
            P("dp"),
            P(),
            P(("row", "col"), "dp"),
            P("dp", None),
            P(),
        ),
        out_specs=P("dp", ("row", "col")),
        check_vma=False,
    )
```

```python
import jax
import jax.numpy as jnp
from jax import lax
from jax.sharding import PartitionSpec as P


def reduce_scatter(x, axis, parts):
    pieces = x.reshape((parts, x.shape[0] // parts) + x.shape[1:])
    got = lax.all_to_all(pieces, axis, 0, 0)
    return jnp.sum(got.astype(jnp.float32), axis=0)


def all_gather(x, axis, parts):
    pieces = jnp.broadcast_to(x[None], (parts,) + x.shape)
    got = lax.all_to_all(pieces, axis, 0, 0)
    return got.reshape((parts * x.shape[0],) + x.shape[1:])


def body(
    hidden_acts,
    out_cotangent,
    is_paraphrase,
    token_edit,
    edit_weight,
    inverse_gram,
    edit_keys,
    edit_slots,
):
    n_dp = lax.axis_size("dp")
    n_rc = lax.axis_size("row") * lax.axis_size("col")
    tokens = hidden_acts.shape[0] * n_dp
    edits = edit_weight.shape[0]
    match = token_edit[:, None] == jnp.arange(edits, dtype=jnp.int32)[None, :]
    looked = jnp.sum(jnp.where(match, edit_weight[None, :], jnp.float32(0.0)), axis=1)
    weight = jnp.where(is_paraphrase == 1, looked, jnp.float32(1.0)) / jnp.sqrt(jnp.float32(tokens))
    scaled = (out_cotangent.astype(jnp.float32) * weight[:, None]).astype(jnp.bfloat16)

    gram_keys = jnp.dot(inverse_gram, edit_keys, preferred_element_type=jnp.float32)
    gram_keys = reduce_scatter(gram_keys.astype(jnp.bfloat16), "dp", n_dp)
    order = (jnp.arange(edits, dtype=jnp.int32)[:, None] == edit_slots[None, :]).astype(jnp.bfloat16)
    gram_keys = jnp.dot(gram_keys.astype(jnp.bfloat16), order, preferred_element_type=jnp.float32).astype(jnp.bfloat16)
    gathered = lax.all_to_all(jnp.broadcast_to(gram_keys[None], (n_dp,) + gram_keys.shape), "dp", 0, 0)
    acts = hidden_acts.reshape(hidden_acts.shape[0], n_dp, hidden_acts.shape[1] // n_dp)
    grad_part = lax.dot_general(scaled, acts, (((0,), (0,)), ((), ())), preferred_element_type=jnp.float32)
    partial = lax.dot_general(
        grad_part.astype(jnp.bfloat16), gathered, (((1, 2), (0, 1)), ((), ())), preferred_element_type=jnp.float32
    )
    slots = partial.shape[1]
    cols = scaled.shape[1]
    partial = partial.reshape(cols, n_dp, slots // n_dp)
    blocks = partial.astype(jnp.bfloat16).transpose(1, 0, 2)
    blocks = blocks.reshape(n_dp * n_rc, 2, (cols // n_rc) * (slots // n_dp) // 2)
    got = lax.all_to_all(blocks, ("dp", "row", "col"), 0, 0)
    total = jnp.sum(got.astype(jnp.float32), axis=0)
    return total.reshape(cols // n_rc, slots // n_dp).T


def solution(mesh):
    return jax.shard_map(
        body,
        mesh=mesh,
        in_specs=(
            P("dp", ("row", "col")),
            P("dp", None),
            P("dp"),
            P("dp"),
            P(),
            P(("row", "col"), "dp"),
            P("dp", None),
            P(),
        ),
        out_specs=P("dp", ("row", "col")),
        check_vma=False,
    )
```

```python
import jax
import jax.numpy as jnp
from jax import lax
from jax.sharding import PartitionSpec as P


def reduce_scatter(x, axis, parts):
    pieces = x.reshape((parts, x.shape[0] // parts) + x.shape[1:])
    got = lax.all_to_all(pieces, axis, 0, 0)
    return jnp.sum(got.astype(jnp.float32), axis=0)


def all_gather(x, axis, parts):
    pieces = jnp.broadcast_to(x[None], (parts,) + x.shape)
    got = lax.all_to_all(pieces, axis, 0, 0)
    return got.reshape((parts * x.shape[0],) + x.shape[1:])


def body(
    hidden_acts,
    out_cotangent,
    is_paraphrase,
    token_edit,
    edit_weight,
    inverse_gram,
    edit_keys,
    edit_slots,
):
    n_dp = lax.axis_size("dp")
    n_rc = lax.axis_size("row") * lax.axis_size("col")
    tokens = hidden_acts.shape[0] * n_dp
    edits = edit_weight.shape[0]
    match = token_edit[:, None] == jnp.arange(edits, dtype=jnp.int32)[None, :]
    looked = jnp.sum(jnp.where(match, edit_weight[None, :], jnp.float32(0.0)), axis=1)
    weight = jnp.where(is_paraphrase == 1, looked, jnp.float32(1.0)) / jnp.sqrt(jnp.float32(tokens))
    scaled = (out_cotangent.astype(jnp.float32) * weight[:, None]).astype(jnp.bfloat16)

    gram_keys = jnp.dot(inverse_gram, edit_keys, preferred_element_type=jnp.float32)
    gram_keys = reduce_scatter(gram_keys.astype(jnp.bfloat16), "dp", n_dp)
    order = (jnp.arange(edits, dtype=jnp.int32)[:, None] == edit_slots[None, :]).astype(jnp.bfloat16)
    gram_keys = jnp.dot(gram_keys.astype(jnp.bfloat16), order, preferred_element_type=jnp.float32).astype(jnp.bfloat16)
    gathered = lax.all_to_all(jnp.broadcast_to(gram_keys[None], (n_dp,) + gram_keys.shape), "dp", 0, 0)
    acts = hidden_acts.reshape(hidden_acts.shape[0], n_dp, hidden_acts.shape[1] // n_dp)
    acts_keys = lax.dot_general(acts, gathered, (((1, 2), (0, 1)), ((), ())), preferred_element_type=jnp.float32)
    slots = acts_keys.shape[1]
    cols = scaled.shape[1]
    partial = lax.dot_general(
        scaled,
        acts_keys.reshape(acts_keys.shape[0], n_dp, slots // n_dp),
        (((0,), (0,)), ((), ())),
        precision=lax.Precision.HIGH,
        preferred_element_type=jnp.float32,
    )
    blocks = partial.astype(jnp.bfloat16).transpose(1, 0, 2)
    blocks = blocks.reshape(n_dp * n_rc, 2, (cols // n_rc) * (slots // n_dp) // 2)
    n_row, n_col = lax.axis_size("row"), lax.axis_size("col")
    core = lax.axis_index("row") % 2
    split = blocks.reshape((n_dp, n_row // 2, 2, n_col) + blocks.shape[1:])
    mine = jnp.take(split, core, axis=2)
    other = jnp.take(split, 1 - core, axis=2)
    other = lax.ppermute(other, "row", [(r, r ^ 1) for r in range(n_row)])
    summed = (mine.astype(jnp.float32) + other.astype(jnp.float32)).astype(jnp.bfloat16)
    summed = summed.reshape((n_dp * n_rc // 2,) + blocks.shape[1:])
    groups = [[m for m in range(n_dp * n_rc) if (m // n_col) % 2 == c] for c in range(2)]
    got = lax.all_to_all(summed, ("dp", "row", "col"), 0, 0, axis_index_groups=groups)
    total = jnp.sum(got.astype(jnp.float32), axis=0)
    return total.reshape(cols // n_rc, slots // n_dp).T


def solution(mesh):
    return jax.shard_map(
        body,
        mesh=mesh,
        in_specs=(
            P("dp", ("row", "col")),
            P("dp", None),
            P("dp"),
            P("dp"),
            P(),
            P(("row", "col"), "dp"),
            P("dp", None),
            P(),
        ),
        out_specs=P("dp", ("row", "col")),
        check_vma=False,
    )
```

```python
import jax
import jax.numpy as jnp
from jax import lax
from jax.sharding import PartitionSpec as P


def reduce_scatter(x, axis, parts):
    pieces = x.reshape((parts, x.shape[0] // parts) + x.shape[1:])
    got = lax.all_to_all(pieces, axis, 0, 0)
    return jnp.sum(got.astype(jnp.float32), axis=0)


def all_gather(x, axis, parts):
    pieces = jnp.broadcast_to(x[None], (parts,) + x.shape)
    got = lax.all_to_all(pieces, axis, 0, 0)
    return got.reshape((parts * x.shape[0],) + x.shape[1:])


def body(
    hidden_acts,
    out_cotangent,
    is_paraphrase,
    token_edit,
    edit_weight,
    inverse_gram,
    edit_keys,
    edit_slots,
):
    n_dp = lax.axis_size("dp")
    n_rc = lax.axis_size("row") * lax.axis_size("col")
    tokens = hidden_acts.shape[0] * n_dp
    edits = edit_weight.shape[0]
    match = token_edit[:, None] == jnp.arange(edits, dtype=jnp.int32)[None, :]
    looked = jnp.sum(jnp.where(match, edit_weight[None, :], jnp.float32(0.0)), axis=1)
    weight = jnp.where(is_paraphrase == 1, looked, jnp.float32(1.0)) / jnp.sqrt(jnp.float32(tokens))
    scaled = (out_cotangent.astype(jnp.float32) * weight[:, None]).astype(jnp.bfloat16)

    gram_keys = jnp.dot(inverse_gram, edit_keys, preferred_element_type=jnp.float32)
    gram_keys = reduce_scatter(gram_keys.astype(jnp.bfloat16), "dp", n_dp)
    order = (jnp.arange(edits, dtype=jnp.int32)[:, None] == edit_slots[None, :]).astype(jnp.bfloat16)
    gram_keys = jnp.dot(gram_keys.astype(jnp.bfloat16), order, preferred_element_type=jnp.float32).astype(jnp.bfloat16)
    gathered = lax.all_to_all(jnp.broadcast_to(gram_keys[None], (n_dp,) + gram_keys.shape), "dp", 0, 0)
    acts = hidden_acts.reshape(hidden_acts.shape[0], n_dp, hidden_acts.shape[1] // n_dp)
    acts_keys = lax.dot_general(acts, gathered, (((1, 2), (0, 1)), ((), ())), preferred_element_type=jnp.float32)
    slots = acts_keys.shape[1]
    cols = scaled.shape[1]
    partial = lax.dot_general(
        scaled,
        acts_keys.reshape(acts_keys.shape[0], n_dp, slots // n_dp),
        (((0,), (0,)), ((), ())),
        precision=lax.Precision.HIGH,
        preferred_element_type=jnp.float32,
    )
    blocks = partial.astype(jnp.bfloat16).transpose(1, 0, 2)
    blocks = blocks.reshape(n_dp * n_rc, 2, (cols // n_rc) * (slots // n_dp) // 2)
    n_row, n_col = lax.axis_size("row"), lax.axis_size("col")
    core = lax.axis_index("row") % 2
    split = blocks.reshape((n_dp, n_row // 2, 2, n_col) + blocks.shape[1:])
    mine = jnp.take(split, core, axis=2)
    other = jnp.take(split, 1 - core, axis=2)
    other = lax.ppermute(other, "row", [(r, r ^ 1) for r in range(n_row)])
    summed = (mine.astype(jnp.float32) + other.astype(jnp.float32)).astype(jnp.bfloat16)
    x_lo = lax.axis_index("row") // 2
    mine = jnp.take(summed, x_lo, axis=1)
    other = jnp.take(summed, 1 - x_lo, axis=1)
    other = lax.ppermute(other, "row", [(r, r ^ 2) for r in range(n_row)])
    summed = (mine.astype(jnp.float32) + other.astype(jnp.float32)).astype(jnp.bfloat16)
    summed = summed.reshape((n_dp * n_col,) + blocks.shape[1:])
    groups = [[m for m in range(n_dp * n_rc) if (m // n_col) % n_row == r] for r in range(n_row)]
    got = lax.all_to_all(summed, ("dp", "row", "col"), 0, 0, axis_index_groups=groups)
    total = jnp.sum(got.astype(jnp.float32), axis=0)
    return total.reshape(cols // n_rc, slots // n_dp).T


def solution(mesh):
    return jax.shard_map(
        body,
        mesh=mesh,
        in_specs=(
            P("dp", ("row", "col")),
            P("dp", None),
            P("dp"),
            P("dp"),
            P(),
            P(("row", "col"), "dp"),
            P("dp", None),
            P(),
        ),
        out_specs=P("dp", ("row", "col")),
        check_vma=False,
    )
```

```python
import jax
import jax.numpy as jnp
from jax import lax
from jax.sharding import PartitionSpec as P


def reduce_scatter(x, axis, parts):
    pieces = x.reshape((parts, x.shape[0] // parts) + x.shape[1:])
    got = lax.all_to_all(pieces, axis, 0, 0)
    return jnp.sum(got.astype(jnp.float32), axis=0)


def all_gather(x, axis, parts):
    pieces = jnp.broadcast_to(x[None], (parts,) + x.shape)
    got = lax.all_to_all(pieces, axis, 0, 0)
    return got.reshape((parts * x.shape[0],) + x.shape[1:])


def body(
    hidden_acts,
    out_cotangent,
    is_paraphrase,
    token_edit,
    edit_weight,
    inverse_gram,
    edit_keys,
    edit_slots,
):
    n_dp = lax.axis_size("dp")
    n_rc = lax.axis_size("row") * lax.axis_size("col")
    tokens = hidden_acts.shape[0] * n_dp
    edits = edit_weight.shape[0]
    match = token_edit[:, None] == jnp.arange(edits, dtype=jnp.int32)[None, :]
    looked = jnp.sum(jnp.where(match, edit_weight[None, :], jnp.float32(0.0)), axis=1)
    weight = jnp.where(is_paraphrase == 1, looked, jnp.float32(1.0)) / jnp.sqrt(jnp.float32(tokens))
    scaled = (out_cotangent.astype(jnp.float32) * weight[:, None]).astype(jnp.bfloat16)

    gram_keys = jnp.dot(inverse_gram, edit_keys, preferred_element_type=jnp.float32)
    gram_keys = reduce_scatter(gram_keys.astype(jnp.bfloat16), "dp", n_dp)
    acts = hidden_acts.reshape(hidden_acts.shape[0], n_dp, hidden_acts.shape[1] // n_dp)
    acts, gram_keys = lax.optimization_barrier((acts, gram_keys))
    order = (jnp.arange(edits, dtype=jnp.int32)[:, None] == edit_slots[None, :]).astype(jnp.bfloat16)
    gram_keys = jnp.dot(gram_keys.astype(jnp.bfloat16), order, preferred_element_type=jnp.float32).astype(jnp.bfloat16)
    gathered = lax.all_to_all(jnp.broadcast_to(gram_keys[None], (n_dp,) + gram_keys.shape), "dp", 0, 0)
    acts_keys = lax.dot_general(acts, gathered, (((1, 2), (0, 1)), ((), ())), preferred_element_type=jnp.float32)
    slots = acts_keys.shape[1]
    cols = scaled.shape[1]
    partial = lax.dot_general(
        scaled,
        acts_keys.reshape(acts_keys.shape[0], n_dp, slots // n_dp),
        (((0,), (0,)), ((), ())),
        precision=lax.Precision.HIGH,
        preferred_element_type=jnp.float32,
    )
    blocks = partial.astype(jnp.bfloat16).transpose(1, 0, 2)
    blocks = blocks.reshape(n_dp * n_rc, 2, (cols // n_rc) * (slots // n_dp) // 2)
    n_row, n_col = lax.axis_size("row"), lax.axis_size("col")
    core = lax.axis_index("row") % 2
    split = blocks.reshape((n_dp, n_row // 2, 2, n_col) + blocks.shape[1:])
    mine = jnp.take(split, core, axis=2)
    other = jnp.take(split, 1 - core, axis=2)
    other = lax.ppermute(other, "row", [(r, r ^ 1) for r in range(n_row)])
    summed = (mine.astype(jnp.float32) + other.astype(jnp.float32)).astype(jnp.bfloat16)
    summed = summed.reshape((n_dp * n_rc // 2,) + blocks.shape[1:])
    groups = [[m for m in range(n_dp * n_rc) if (m // n_col) % 2 == c] for c in range(2)]
    got = lax.all_to_all(summed, ("dp", "row", "col"), 0, 0, axis_index_groups=groups)
    total = jnp.sum(got.astype(jnp.float32), axis=0)
    return total.reshape(cols // n_rc, slots // n_dp).T


def solution(mesh):
    return jax.shard_map(
        body,
        mesh=mesh,
        in_specs=(
            P("dp", ("row", "col")),
            P("dp", None),
            P("dp"),
            P("dp"),
            P(),
            P(("row", "col"), "dp"),
            P("dp", None),
            P(),
        ),
        out_specs=P("dp", ("row", "col")),
        check_vma=False,
    )
```

```python
import jax
import jax.numpy as jnp
from jax import lax
from jax.sharding import PartitionSpec as P


def reduce_scatter(x, axis, parts):
    pieces = x.reshape((parts, x.shape[0] // parts) + x.shape[1:])
    got = lax.all_to_all(pieces, axis, 0, 0)
    return jnp.sum(got.astype(jnp.float32), axis=0)


def all_gather(x, axis, parts):
    pieces = jnp.broadcast_to(x[None], (parts,) + x.shape)
    got = lax.all_to_all(pieces, axis, 0, 0)
    return got.reshape((parts * x.shape[0],) + x.shape[1:])


def body(
    hidden_acts,
    out_cotangent,
    is_paraphrase,
    token_edit,
    edit_weight,
    inverse_gram,
    edit_keys,
    edit_slots,
):
    n_dp = lax.axis_size("dp")
    n_rc = lax.axis_size("row") * lax.axis_size("col")
    tokens = hidden_acts.shape[0] * n_dp
    edits = edit_weight.shape[0]
    match = token_edit[:, None] == jnp.arange(edits, dtype=jnp.int32)[None, :]
    looked = jnp.sum(jnp.where(match, edit_weight[None, :], jnp.float32(0.0)), axis=1)
    weight = jnp.where(is_paraphrase == 1, looked, jnp.float32(1.0)) / jnp.sqrt(jnp.float32(tokens))
    scaled = (out_cotangent.astype(jnp.float32) * weight[:, None]).astype(jnp.bfloat16)

    gram_keys = jnp.dot(inverse_gram, edit_keys, preferred_element_type=jnp.float32)
    gram_keys = reduce_scatter(gram_keys.astype(jnp.bfloat16), "dp", n_dp)
    order = (jnp.arange(edits, dtype=jnp.int32)[:, None] == edit_slots[None, :]).astype(jnp.bfloat16)
    copies = jnp.broadcast_to(gram_keys.astype(jnp.bfloat16)[None], (n_dp,) + gram_keys.shape)
    copies = jnp.dot(copies, order, preferred_element_type=jnp.float32).astype(jnp.bfloat16)
    gathered = lax.all_to_all(copies, "dp", 0, 0)
    acts = hidden_acts.reshape(hidden_acts.shape[0], n_dp, hidden_acts.shape[1] // n_dp)
    acts_keys = lax.dot_general(acts, gathered, (((1, 2), (0, 1)), ((), ())), preferred_element_type=jnp.float32)
    slots = acts_keys.shape[1]
    cols = scaled.shape[1]
    partial = lax.dot_general(
        scaled,
        acts_keys.reshape(acts_keys.shape[0], n_dp, slots // n_dp),
        (((0,), (0,)), ((), ())),
        precision=lax.Precision.HIGH,
        preferred_element_type=jnp.float32,
    )
    blocks = partial.astype(jnp.bfloat16).transpose(1, 0, 2)
    blocks = blocks.reshape(n_dp * n_rc, 2, (cols // n_rc) * (slots // n_dp) // 2)
    n_row, n_col = lax.axis_size("row"), lax.axis_size("col")
    core = lax.axis_index("row") % 2
    split = blocks.reshape((n_dp, n_row // 2, 2, n_col) + blocks.shape[1:])
    mine = jnp.take(split, core, axis=2)
    other = jnp.take(split, 1 - core, axis=2)
    other = lax.ppermute(other, "row", [(r, r ^ 1) for r in range(n_row)])
    summed = (mine.astype(jnp.float32) + other.astype(jnp.float32)).astype(jnp.bfloat16)
    summed = summed.reshape((n_dp * n_rc // 2,) + blocks.shape[1:])
    groups = [[m for m in range(n_dp * n_rc) if (m // n_col) % 2 == c] for c in range(2)]
    got = lax.all_to_all(summed, ("dp", "row", "col"), 0, 0, axis_index_groups=groups)
    total = jnp.sum(got.astype(jnp.float32), axis=0)
    return total.reshape(cols // n_rc, slots // n_dp).T


def solution(mesh):
    return jax.shard_map(
        body,
        mesh=mesh,
        in_specs=(
            P("dp", ("row", "col")),
            P("dp", None),
            P("dp"),
            P("dp"),
            P(),
            P(("row", "col"), "dp"),
            P("dp", None),
            P(),
        ),
        out_specs=P("dp", ("row", "col")),
        check_vma=False,
    )
```
